256 devices in a mesh: grp: 8 (over z_lo, core), ep: 32 (over z_hi, y, x).
Axes of the slice: x: 4, y: 4, z: 8 (z_hi: 2, z_lo: 4; z = z_hi * 4 + z_lo), core: 2. Of those that a mesh axis runs over, the one named last changes fastest.
Arguments:
- tokens_in: bfloat16 [32768, 2048], P(('grp', 'ep')), may hold values from -6 to 6
- grad_out: bfloat16 [32768, 2048], P(('grp', 'ep')), may hold values from -6 to 6
- replica_of: int32 [32768, 2], P(('grp', 'ep')), may hold values from 0 to 255, all different within a row; in each aligned block of 128 rows (0 to 127, 128 to 255, ...) at most 2 rows name the same one
- gate_weights: bfloat16 [32768, 2], P(('grp', 'ep')), may hold values from 0.099609375 to 1
- placement: int32 [8, 32], replicated, may hold values from 0 to 1, as said below
- w_in_rep: bfloat16 [8, 32, 2048, 1024], P('grp', 'ep'), as said below
- w_down_rep: bfloat16 [8, 32, 2048, 512], P('grp', 'ep'), as said below
Outputs:
- d_tokens: bfloat16 [32768, 2048], P(('grp', 'ep'))
- d_gates: bfloat16 [32768, 2], P(('grp', 'ep'))
- grad_in: bfloat16 [64, 2048, 1024], P('ep', 'grp')
- grad_down: bfloat16 [64, 2048, 512], P('ep', 'grp')
The draws below stay inside these ranges and needn't reach their ends.
Inputs may be any that keep to these rules, and one draw needn't show every extreme that they name: `replica_of`: A row names a replica device by its index in the order grp then ep. The 2 rows of a token name different devices. At most 2 of the rows of one device name the same replica device, and some device sends exactly 2 rows to one replica. placement[g, e] selects expert e * 2 + placement[g, e]; in every column e each of the 2 values occurs at least once, so every expert has at least one copy. w_in_rep[g, e] and w_in_rep[g2, e] are equal wherever placement[g, e] equals placement[g2, e]. w_down_rep[g, e] and w_down_rep[g2, e] are equal wherever placement[g, e] equals placement[g2, e].
All inputs are finite; a program needn't handle non-finite values.
Results may differ from the reference program's by a relative error of at most 0.01.
Values may be sent and summed in bfloat16 or wider, within the bound.
No kernel may reach another device: no remote copies, remote signals or barrier semaphores. Data moves between devices by JAX's collectives and lax.ppermute only.
A program may use at most 128 MiB of HBM per device.

```python
import math
import jax
import jax.numpy as jnp
import numpy as np
from jax import lax

D = 2048
H = 512
KPC = 2
TOP = 2
TOK_DEV = 128
EXPERTS = 64
TOKENS = 32768
CAP = 2
N_GRP = 8
N_EP = 32


def placement_plan(key):
    keys = jax.random.split(key, N_EP + 1)
    counts = jax.random.randint(keys[0], (N_EP,), 1, N_GRP)
    orders = jax.vmap(lambda single: jax.random.permutation(single, N_GRP))(keys[1:])
    plan = (orders >= counts[:, None]).astype(jnp.int32)
    return plan.T


def copies_of(key, canon):
    plan = placement_plan(jax.random.fold_in(key, 11))
    expert = jnp.arange(N_EP, dtype=jnp.int32)[None, :] * KPC + plan
    return canon[expert]


def draw_placement(key, part):
    return placement_plan(jax.random.fold_in(key, 11))


def draw_w_in_rep(key, part):
    inner = jax.random.fold_in(key, 23)
    canon = jax.random.normal(inner, (EXPERTS, D, 2 * H), jnp.float32) * D ** (-0.5)
    return copies_of(key, canon.astype(jnp.bfloat16))


def draw_w_down_rep(key, part):
    inner = jax.random.fold_in(key, 37)
    canon = jax.random.normal(inner, (EXPERTS, D, H), jnp.float32) * H ** (-0.5)
    return copies_of(key, canon.astype(jnp.bfloat16))


def levels(rng, shape, shards, smallest, largest):
    factor_of, own = 1.0, jax.random.fold_in(rng, 6)
    for axis_at, blocks in shards:
        heights = jnp.exp(jax.random.uniform(jax.random.fold_in(own, axis_at), (blocks,), jnp.float32, smallest / len(shards), largest / len(shards)))
        factor_of = factor_of * jnp.repeat(heights, shape[axis_at] // blocks).reshape([-1 if axis == axis_at else 1 for axis in range(len(shape))])
    return factor_of


def assign_block(key, own, number, rows, number_of, top, reach, skew):
    ranking = jax.random.permutation(key, number_of)
    packed, common = shares(number_of, rows * top, reach, skew, True), shares(number_of, rows * top, reach, skew, False)
    places = jnp.arange(number_of)

    def named(lengths, turn):
        used = int((lengths > 0).sum())
        fixed = max(1, used // 4)
        passed = fixed + (places - fixed + turn * (used - fixed)) % max(1, number_of - fixed)
        return jnp.zeros((number_of,), jnp.int32).at[ranking[jnp.where(places < fixed, places, passed)]].set(jnp.asarray(lengths, jnp.int32))

    lengths = jnp.where(number % 4 == 0, named(packed, number // 4), named(common, number - number // 4 - 1))
    mixed = jax.random.permutation(jax.random.fold_in(own, 3), number_of)
    giver, taker = mixed[0:number_of // 2 * 2:2], mixed[1:number_of // 2 * 2:2]
    margin = jnp.minimum(lengths[giver] - 1, reach - lengths[taker]) // 2
    margin = jnp.where((giver == ranking[0]) | (taker == ranking[0]) | (lengths[taker] == 0), 0, jnp.maximum(margin, 0))
    passed = jax.random.randint(jax.random.fold_in(own, 4), (number_of // 2,), 0, 1 << 20) % (margin + 1)
    lengths = lengths.at[giver].add(-passed).at[taker].add(passed)
    labels = jnp.searchsorted(jnp.cumsum(lengths), jnp.arange(rows * top), side="right").astype(jnp.int32)
    listing = labels.reshape(top, rows).T
    listing = listing[jax.random.permutation(jax.random.fold_in(own, 1), rows)]
    turn = jax.random.randint(jax.random.fold_in(own, 2), (rows, 1), 0, top)
    return jnp.take_along_axis(listing, (jnp.arange(top)[None, :] + turn) % top, axis=1)


def shares(amount, total, bound, lean, full):
    portions = [(1 << 20) // math.isqrt(standing ** lean) + 1 for standing in range(1, amount + 1)]
    largest = bound if full else min(bound, max(-(-total // amount), total * portions[0] // sum(portions)))
    least = 1 if total - largest >= amount - 1 else 0
    holding, surplus = [largest] + [least] * (amount - 1), total - largest - least * (amount - 1)
    while surplus > 0:
        movable = [i for i in range(1, amount) if holding[i] < largest] or [i for i in range(1, amount) if holding[i] < bound]
        mass, remaining = sum([portions[i] for i in movable]), surplus
        for i in movable:
            more = min(bound - holding[i], max(1, remaining * portions[i] // mass), surplus)
            holding[i] = holding[i] + more
            surplus = surplus - more
    return np.array(holding)


def bell_draw(key, shape, width, most, cuts=(), kind=jnp.bfloat16):
    gain = levels(key, shape, cuts, -0.22, 0.18) if cuts else 1.0
    array = jax.random.normal(key, shape, jnp.float32) * width * gain
    return jnp.minimum(jnp.maximum(array, -most), most).astype(kind)


def setup_inputs(seed: int = 0) -> dict:
    key_of = jax.random.split(jax.random.key(seed), 8)
    tokens_in = bell_draw(key_of[0], (TOKENS, D), 1.0, 6.0, ((0, 256),))
    grad_out = bell_draw(key_of[1], (TOKENS, D), 1.0, 6.0, ((0, 256),))
    replica_of_keys = jax.random.split(jax.random.fold_in(key_of[2], 1), TOKENS // TOK_DEV)
    replica_of_turns = jax.random.permutation(jax.random.fold_in(key_of[2], 3), TOKENS // TOK_DEV)
    replica_of = jax.vmap(lambda own, number: assign_block(jax.random.fold_in(key_of[2], 2), own, number, TOK_DEV, N_GRP * N_EP, TOP, CAP, 2))(replica_of_keys, replica_of_turns).reshape((TOKENS, TOP))
    gate_weights = jnp.clip(0.099609375 + 0.9003906 * jax.random.uniform(key_of[3], (TOKENS, TOP), jnp.float32) ** levels(key_of[3], (TOKENS, TOP), ((0, 256),), -0.2, 0.2), 0.099609375, 1.0).astype(jnp.bfloat16)
    placement = draw_placement(jax.random.fold_in(key_of[7], 71), 0)
    w_in_rep = draw_w_in_rep(jax.random.fold_in(key_of[7], 71), 0)
    w_down_rep = draw_w_down_rep(jax.random.fold_in(key_of[7], 71), 0)
    return {"tokens_in": tokens_in, "grad_out": grad_out, "replica_of": replica_of, "gate_weights": gate_weights, "placement": placement, "w_in_rep": w_in_rep, "w_down_rep": w_down_rep}


def expert_backward(rows_x, rows_dy, rows_gate, w_in, w_down):
    hidden = w_down.shape[1]
    both = jnp.dot(rows_x, w_in, preferred_element_type=jnp.float32)
    gate_pre = both[:, :hidden]
    up_part = both[:, hidden:]
    sigmoid_gate = jax.nn.sigmoid(gate_pre)
    silu_gate = gate_pre * sigmoid_gate
    activation = (silu_gate * up_part).astype(jnp.bfloat16)
    out_rows = lax.dot_general(activation, w_down, (((1,), (1,)), ((), ())), preferred_element_type=jnp.float32)
    gate_grad = jnp.sum(rows_dy.astype(jnp.float32) * out_rows, axis=1).astype(jnp.bfloat16)
    out_grad = (rows_gate.astype(jnp.float32)[:, None] * rows_dy.astype(jnp.float32)).astype(jnp.bfloat16)
    act_grad = jnp.dot(out_grad, w_down, preferred_element_type=jnp.float32)
    gate_grad_pre = act_grad * up_part * sigmoid_gate * (1.0 + gate_pre * (1.0 - sigmoid_gate))
    up_grad = act_grad * silu_gate
    both_grad = jnp.concatenate([gate_grad_pre, up_grad], axis=1).astype(jnp.bfloat16)
    row_grad = lax.dot_general(both_grad, w_in, (((1,), (1,)), ((), ())), preferred_element_type=jnp.float32).astype(jnp.bfloat16)
    part_in = lax.dot_general(rows_x, both_grad, (((0,), (0,)), ((), ())), preferred_element_type=jnp.float32)
    part_down = lax.dot_general(out_grad, activation, (((0,), (0,)), ((), ())), preferred_element_type=jnp.float32)
    return row_grad, gate_grad, part_in, part_down


def reference(tokens_in, grad_out, replica_of, gate_weights, placement, w_in_rep, w_down_rep):
    devices = N_GRP * N_EP
    per_device = TOK_DEV * TOP
    dest_rows = replica_of.reshape(devices, per_device)
    order_ids = jnp.arange(per_device, dtype=jnp.int32)

    def ranks(row_dest):
        earlier = (row_dest[:, None] == row_dest[None, :]) & (order_ids[None, :] < order_ids[:, None])
        return jnp.sum(earlier.astype(jnp.int32), axis=1).astype(jnp.int32)

    rank_in = lax.map(ranks, dest_rows)
    sources = jnp.arange(devices, dtype=jnp.int32)[:, None]
    global_slot = (dest_rows * (devices * CAP) + sources * CAP + rank_in).reshape(-1).astype(jnp.int32)
    row_ids = jnp.arange(devices * per_device, dtype=jnp.int32)
    slot_table = jnp.full((devices * devices * CAP,), -1, jnp.int32).at[global_slot].set(row_ids)
    flat_gate = gate_weights.reshape(-1)

    def step(carry, replica):
        acc_in, acc_down = carry
        start = (replica * devices * CAP).astype(jnp.int32)
        ids = lax.dynamic_slice(slot_table, (start,), (devices * CAP,))
        is_live = ids >= 0
        safe_ids = jnp.maximum(ids, 0)
        token_ids = safe_ids // TOP
        rows_x = jnp.where(is_live[:, None], tokens_in[token_ids], jnp.zeros((), tokens_in.dtype))
        rows_dy = jnp.where(is_live[:, None], grad_out[token_ids], jnp.zeros((), grad_out.dtype))
        rows_gate = jnp.where(is_live, flat_gate[safe_ids], jnp.zeros((), gate_weights.dtype))
        group = replica // N_EP
        column = replica % N_EP
        expert = column * KPC + placement[group, column]
        row_grad, gate_grad, part_in, part_down = expert_backward(rows_x, rows_dy, rows_gate, w_in_rep[group, column], w_down_rep[group, column])
        part_in = lax.optimization_barrier(part_in.astype(jnp.bfloat16)).astype(jnp.float32)
        part_down = lax.optimization_barrier(part_down.astype(jnp.bfloat16)).astype(jnp.float32)
        acc_in = acc_in.at[expert].add(part_in)
        acc_down = acc_down.at[expert].add(part_down)
        return (acc_in, acc_down), (row_grad, gate_grad)

    init = (jnp.zeros((EXPERTS, D, 2 * H), jnp.float32), jnp.zeros((EXPERTS, D, H), jnp.float32))
    (acc_in, acc_down), (all_rows, all_gates) = lax.scan(step, init, jnp.arange(devices, dtype=jnp.int32))
    row_grads = all_rows.reshape(-1, D)[global_slot]
    d_tokens = jnp.sum(row_grads.reshape(TOKENS, TOP, D).astype(jnp.float32), axis=1).astype(jnp.bfloat16)
    d_gates = all_gates.reshape(-1)[global_slot].reshape(TOKENS, TOP)
    return d_tokens, d_gates, acc_in.astype(jnp.bfloat16), acc_down.astype(jnp.bfloat16)
```

```python
import jax
import jax.numpy as jnp
from jax import lax
from jax.sharding import PartitionSpec as P

KPC = 2


def expert_backward(rows_x, rows_dy, rows_gate, w_in, w_down):
    hidden = w_down.shape[1]
    both = jnp.dot(rows_x, w_in, preferred_element_type=jnp.float32)
    gate_pre = both[:, :hidden]
    up_part = both[:, hidden:]
    sigmoid_gate = jax.nn.sigmoid(gate_pre)
    silu_gate = gate_pre * sigmoid_gate
    activation = (silu_gate * up_part).astype(jnp.bfloat16)
    out_rows = lax.dot_general(
        activation, w_down, (((1,), (1,)), ((), ())), preferred_element_type=jnp.float32
    )
    gate_grad = jnp.sum(rows_dy.astype(jnp.float32) * out_rows, axis=1).astype(jnp.bfloat16)
    out_grad = (rows_gate.astype(jnp.float32)[:, None] * rows_dy.astype(jnp.float32)).astype(
        jnp.bfloat16
    )
    act_grad = jnp.dot(out_grad, w_down, preferred_element_type=jnp.float32)
    gate_grad_pre = act_grad * up_part * sigmoid_gate * (1.0 + gate_pre * (1.0 - sigmoid_gate))
    up_grad = act_grad * silu_gate
    both_grad = jnp.concatenate([gate_grad_pre, up_grad], axis=1).astype(jnp.bfloat16)
    row_grad = lax.dot_general(
        both_grad, w_in, (((1,), (1,)), ((), ())), preferred_element_type=jnp.float32
    ).astype(jnp.bfloat16)
    part_in = lax.dot_general(
        rows_x, both_grad, (((0,), (0,)), ((), ())), preferred_element_type=jnp.float32
    )
    part_down = lax.dot_general(
        out_grad, activation, (((0,), (0,)), ((), ())), preferred_element_type=jnp.float32
    )
    return (row_grad, gate_grad, part_in, part_down)


def shards(tokens_in, grad_out, replica_of, gate_weights, placement, w_in_rep, w_down_rep):
    tok_count, model_width = tokens_in.shape
    top_count = replica_of.shape[1]
    group_count = lax.axis_size("grp")
    lane_count = lax.axis_size("ep")
    device_count = group_count * lane_count
    capacity = max(2, 2 * tok_count * top_count // device_count)
    w_in = w_in_rep[0, 0]
    w_down = w_down_rep[0, 0]
    dest_rows = replica_of.reshape(-1)
    row_count = tok_count * top_count
    row_ids = jnp.arange(row_count, dtype=jnp.int32)
    earlier = (dest_rows[:, None] == dest_rows[None, :]) & (row_ids[None, :] < row_ids[:, None])
    rank_in = jnp.sum(earlier.astype(jnp.int32), axis=1)
    send_slot = dest_rows * capacity + rank_in
    slot_table = jnp.full((device_count * capacity,), -1, jnp.int32).at[send_slot].set(row_ids)
    is_live = slot_table >= 0
    safe_ids = jnp.maximum(slot_table, 0)
    token_ids = safe_ids // top_count
    send_x = jnp.where(is_live[:, None], tokens_in[token_ids], jnp.zeros((), tokens_in.dtype))
    send_dy = jnp.where(is_live[:, None], grad_out[token_ids], jnp.zeros((), grad_out.dtype))
    send_gate = jnp.where(
        is_live, gate_weights.reshape(-1)[safe_ids], jnp.zeros((), gate_weights.dtype)
    )
    lane_pad = 128
    gate_cols = jnp.zeros((device_count * capacity, lane_pad), send_x.dtype).at[:, 0].set(send_gate)
    outgoing = jnp.concatenate([send_x, send_dy, gate_cols], axis=1).reshape(
        device_count, capacity, 2 * model_width + lane_pad
    )
    arrived = lax.all_to_all(outgoing, ("grp", "ep"), 0, 0, tiled=True).reshape(
        device_count * capacity, 2 * model_width + lane_pad
    )
    rows_x = arrived[:, :model_width]
    rows_dy = arrived[:, model_width : 2 * model_width]
    rows_gate = arrived[:, 2 * model_width]
    row_grad, gate_grad, part_in, part_down = expert_backward(
        rows_x, rows_dy, rows_gate, w_in, w_down
    )
    back_cols = jnp.zeros((device_count * capacity, lane_pad), row_grad.dtype).at[:, 0].set(gate_grad)
    returning = jnp.concatenate([row_grad, back_cols], axis=1).reshape(
        device_count, capacity, model_width + lane_pad
    )
    came_back = lax.all_to_all(returning, ("grp", "ep"), 0, 0, tiled=True).reshape(
        device_count * capacity, model_width + lane_pad
    )[send_slot]
    grads_rows = came_back[:, :model_width]
    d_tokens = jnp.sum(
        grads_rows.reshape(tok_count, top_count, model_width).astype(jnp.float32), axis=1
    ).astype(jnp.bfloat16)
    d_gates = came_back[:, model_width].reshape(tok_count, top_count)
    group_index = lax.axis_index("grp")
    column_index = lax.axis_index("ep")
    my_slot = placement[group_index, column_index]
    slot_mask = (jnp.arange(KPC, dtype=jnp.int32) == my_slot).astype(jnp.float32)
    stack_in = slot_mask[:, None, None] * part_in[None]
    stack_down = slot_mask[:, None, None] * part_down[None]
    summed_in, summed_down = (
        lax.psum_scatter(
            stack_in.astype(jnp.bfloat16), "grp", scatter_dimension=1, tiled=True
        ).astype(jnp.float32),
        lax.psum_scatter(
            stack_down.astype(jnp.bfloat16), "grp", scatter_dimension=1, tiled=True
        ).astype(jnp.float32),
    )
    return (d_tokens, d_gates, summed_in.astype(jnp.bfloat16), summed_down.astype(jnp.bfloat16))


def solution(mesh):
    placed = (
        P(("grp", "ep"), None),
        P(("grp", "ep"), None),
        P(("grp", "ep"), None),
        P(("grp", "ep"), None),
        P(),
        P("grp", "ep", None, None),
        P("grp", "ep", None, None),
    )
    return jax.shard_map(
        shards,
        mesh=mesh,
        in_specs=placed,
        out_specs=(
            P(("grp", "ep"), None),
            P(("grp", "ep"), None),
            P("ep", "grp", None),
            P("ep", "grp", None),
        ),
        check_vma=False,
    )
```

```python
import jax
import jax.numpy as jnp
from jax import lax
from jax.sharding import PartitionSpec as P

KPC = 2


def expert_backward(rows_x, rows_dy, rows_gate, w_in, w_down):
    hidden = w_down.shape[1]
    both = jnp.dot(rows_x, w_in, preferred_element_type=jnp.float32)
    gate_pre = both[:, :hidden]
    up_part = both[:, hidden:]
    sigmoid_gate = jax.nn.sigmoid(gate_pre)
    silu_gate = gate_pre * sigmoid_gate
    activation = (silu_gate * up_part).astype(jnp.bfloat16)
    out_rows = lax.dot_general(
        activation, w_down, (((1,), (1,)), ((), ())), preferred_element_type=jnp.float32
    )
    gate_grad = jnp.sum(rows_dy.astype(jnp.float32) * out_rows, axis=1).astype(jnp.bfloat16)
    out_grad = (rows_gate.astype(jnp.float32)[:, None] * rows_dy.astype(jnp.float32)).astype(
        jnp.bfloat16
    )
    act_grad = jnp.dot(out_grad, w_down, preferred_element_type=jnp.float32)
    gate_grad_pre = act_grad * up_part * sigmoid_gate * (1.0 + gate_pre * (1.0 - sigmoid_gate))
    up_grad = act_grad * silu_gate
    both_grad = jnp.concatenate([gate_grad_pre, up_grad], axis=1).astype(jnp.bfloat16)
    row_grad = lax.dot_general(
        both_grad, w_in, (((1,), (1,)), ((), ())), preferred_element_type=jnp.float32
    ).astype(jnp.bfloat16)
    part_in = lax.dot_general(
        rows_x, both_grad, (((0,), (0,)), ((), ())), preferred_element_type=jnp.float32
    )
    part_down = lax.dot_general(
        out_grad, activation, (((0,), (0,)), ((), ())), preferred_element_type=jnp.float32
    )
    return (row_grad, gate_grad, part_in, part_down)


def shards(tokens_in, grad_out, replica_of, gate_weights, placement, w_in_rep, w_down_rep):
    tok_count, model_width = tokens_in.shape
    top_count = replica_of.shape[1]
    group_count = lax.axis_size("zl") * lax.axis_size("core")
    lane_count = lax.axis_size("ep")
    device_count = group_count * lane_count
    capacity = max(2, 2 * tok_count * top_count // device_count)
    w_in = w_in_rep[0, 0]
    w_down = w_down_rep[0, 0]
    dest_rows = replica_of.reshape(-1)
    row_count = tok_count * top_count
    row_ids = jnp.arange(row_count, dtype=jnp.int32)
    earlier = (dest_rows[:, None] == dest_rows[None, :]) & (row_ids[None, :] < row_ids[:, None])
    rank_in = jnp.sum(earlier.astype(jnp.int32), axis=1)
    send_slot = dest_rows * capacity + rank_in
    slot_table = jnp.full((device_count * capacity,), -1, jnp.int32).at[send_slot].set(row_ids)
    is_live = slot_table >= 0
    safe_ids = jnp.maximum(slot_table, 0)
    token_ids = safe_ids // top_count
    send_x = jnp.where(is_live[:, None], tokens_in[token_ids], jnp.zeros((), tokens_in.dtype))
    send_dy = jnp.where(is_live[:, None], grad_out[token_ids], jnp.zeros((), grad_out.dtype))
    send_gate = jnp.where(
        is_live, gate_weights.reshape(-1)[safe_ids], jnp.zeros((), gate_weights.dtype)
    )
    lane_pad = 128
    gate_cols = jnp.zeros((device_count * capacity, lane_pad), send_x.dtype).at[:, 0].set(send_gate)
    outgoing = jnp.concatenate([send_x, send_dy, gate_cols], axis=1).reshape(
        device_count, capacity, 2 * model_width + lane_pad
    )
    arrived = lax.all_to_all(outgoing, ("zl", "core", "ep"), 0, 0, tiled=True).reshape(
        device_count * capacity, 2 * model_width + lane_pad
    )
    rows_x = arrived[:, :model_width]
    rows_dy = arrived[:, model_width : 2 * model_width]
    rows_gate = arrived[:, 2 * model_width]
    row_grad, gate_grad, part_in, part_down = expert_backward(
        rows_x, rows_dy, rows_gate, w_in, w_down
    )
    back_cols = jnp.zeros((device_count * capacity, lane_pad), row_grad.dtype).at[:, 0].set(gate_grad)
    returning = jnp.concatenate([row_grad, back_cols], axis=1).reshape(
        device_count, capacity, model_width + lane_pad
    )
    came_back = lax.all_to_all(returning, ("zl", "core", "ep"), 0, 0, tiled=True).reshape(
        device_count * capacity, model_width + lane_pad
    )[send_slot]
    grads_rows = came_back[:, :model_width]
    d_tokens = jnp.sum(
        grads_rows.reshape(tok_count, top_count, model_width).astype(jnp.float32), axis=1
    ).astype(jnp.bfloat16)
    d_gates = came_back[:, model_width].reshape(tok_count, top_count)
    core_count = lax.axis_size("core")
    core_index = lax.axis_index("core")
    group_index = lax.axis_index("zl") * core_count + core_index
    column_index = lax.axis_index("ep")
    partner_index = group_index - core_index + (core_count - 1 - core_index)
    own_slot = placement[group_index, column_index]
    partner_slot = placement[partner_index, column_index]
    hidden_width = part_down.shape[1]
    parts = jnp.concatenate([part_in, part_down], axis=1).astype(jnp.bfloat16)
    parts = parts.reshape(-1, core_count, model_width // group_count, parts.shape[1])
    own_rows = jnp.take(parts, core_index, axis=1)
    send_rows = jnp.take(parts, core_count - 1 - core_index, axis=1)
    got_rows = lax.ppermute(send_rows, "core", [(0, 1), (1, 0)])
    slots = jnp.arange(KPC, dtype=jnp.int32)
    own_mask = (slots == own_slot).astype(jnp.float32)[:, None, None, None]
    got_mask = (slots == partner_slot).astype(jnp.float32)[:, None, None, None]
    stacked = (
        own_mask * own_rows[None].astype(jnp.float32) + got_mask * got_rows[None].astype(jnp.float32)
    ).astype(jnp.bfloat16)
    summed = lax.psum_scatter(stacked, "zl", scatter_dimension=1, tiled=True)
    summed = summed.reshape(KPC, model_width // group_count, -1)
    width_in = summed.shape[2] - hidden_width
    return (d_tokens, d_gates, summed[:, :, :width_in], summed[:, :, width_in:])


def solution(mesh):
    grp_size = mesh.shape["grp"]
    core_size = 2
    split_mesh = jax.sharding.Mesh(
        mesh.devices.reshape(grp_size // core_size, core_size, mesh.shape["ep"]), ("zl", "core", "ep")
    )
    rows = ("zl", "core", "ep")
    placed = (
        P(rows, None),
        P(rows, None),
        P(rows, None),
        P(rows, None),
        P(),
        P(("zl", "core"), "ep", None, None),
        P(("zl", "core"), "ep", None, None),
    )
    return jax.shard_map(
        shards,
        mesh=split_mesh,
        in_specs=placed,
        out_specs=(
            P(rows, None),
            P(rows, None),
            P("ep", ("zl", "core"), None),
            P("ep", ("zl", "core"), None),
        ),
        check_vma=False,
    )
```

```python
import jax
import jax.numpy as jnp
from jax import lax
from jax.sharding import PartitionSpec as P

KPC = 2


def expert_backward(rows_x, rows_dy, rows_gate, w_in, w_down):
    hidden = w_down.shape[1]
    both = jnp.dot(rows_x, w_in, preferred_element_type=jnp.float32)
    gate_pre = both[:, :hidden]
    up_part = both[:, hidden:]
    sigmoid_gate = jax.nn.sigmoid(gate_pre)
    silu_gate = gate_pre * sigmoid_gate
    activation = (silu_gate * up_part).astype(jnp.bfloat16)
    out_rows = lax.dot_general(
        activation, w_down, (((1,), (1,)), ((), ())), preferred_element_type=jnp.float32
    )
    gate_grad = jnp.sum(rows_dy.astype(jnp.float32) * out_rows, axis=1).astype(jnp.bfloat16)
    out_grad = (rows_gate.astype(jnp.float32)[:, None] * rows_dy.astype(jnp.float32)).astype(
        jnp.bfloat16
    )
    act_grad = jnp.dot(out_grad, w_down, preferred_element_type=jnp.float32)
    gate_grad_pre = act_grad * up_part * sigmoid_gate * (1.0 + gate_pre * (1.0 - sigmoid_gate))
    up_grad = act_grad * silu_gate
    both_grad = jnp.concatenate([gate_grad_pre, up_grad], axis=1).astype(jnp.bfloat16)
    row_grad = lax.dot_general(
        both_grad, w_in, (((1,), (1,)), ((), ())), preferred_element_type=jnp.float32
    ).astype(jnp.bfloat16)
    part_in = lax.dot_general(
        rows_x, both_grad, (((0,), (0,)), ((), ())), preferred_element_type=jnp.float32
    )
    part_down = lax.dot_general(
        out_grad, activation, (((0,), (0,)), ((), ())), preferred_element_type=jnp.float32
    )
    return (row_grad, gate_grad, part_in, part_down)


def shards(tokens_in, grad_out, replica_of, gate_weights, placement, w_in_rep, w_down_rep):
    tok_count, model_width = tokens_in.shape
    top_count = replica_of.shape[1]
    group_count = lax.axis_size("zl") * lax.axis_size("core")
    lane_count = lax.axis_size("ep")
    device_count = group_count * lane_count
    capacity = max(2, 2 * tok_count * top_count // device_count)
    w_in = w_in_rep[0, 0]
    w_down = w_down_rep[0, 0]
    dest_rows = replica_of.reshape(-1)
    row_count = tok_count * top_count
    row_ids = jnp.arange(row_count, dtype=jnp.int32)
    core_count = lax.axis_size("core")
    line_count = group_count // core_count
    ring_count = 2 * line_count
    my_group = lax.axis_index("zl") * core_count + lax.axis_index("core")
    my_column = lax.axis_index("ep")
    groups = jnp.arange(group_count, dtype=jnp.int32)
    columns = jnp.arange(lane_count, dtype=jnp.int32)
    z_of = (columns[None, :] // (lane_count // 2)) * line_count + (groups[:, None] // core_count)
    my_z = (my_column // (lane_count // 2)) * line_count + my_group // core_count
    hops = jnp.abs(z_of - my_z) % ring_count
    hops = jnp.minimum(hops, ring_count - hops)
    key = hops * (2 * group_count) + (groups[:, None] != my_group) * group_count + groups[:, None]
    dest_group = dest_rows // lane_count
    dest_column = dest_rows % lane_count
    dest_expert = placement[dest_group, dest_column]
    is_copy = placement[:, dest_column].T == dest_expert[:, None]
    row_key = jnp.where(is_copy, key[:, dest_column].T, jnp.int32(1 << 20))
    place = jnp.sum((row_key[:, None, :] < row_key[:, :, None]).astype(jnp.int32), axis=2)
    expert_id = dest_column * KPC + dest_expert
    earlier = (expert_id[:, None] == expert_id[None, :]) & (row_ids[None, :] < row_ids[:, None])
    rank_in = jnp.sum(earlier.astype(jnp.int32), axis=1)
    pick = is_copy & (place == (rank_in // capacity)[:, None])
    new_group = jnp.sum(jnp.where(pick, groups[None, :], 0), axis=1)
    send_slot = (new_group * lane_count + dest_column) * capacity + rank_in % capacity
    slot_table = jnp.full((device_count * capacity,), -1, jnp.int32).at[send_slot].set(row_ids)
    is_live = slot_table >= 0
    safe_ids = jnp.maximum(slot_table, 0)
    token_ids = safe_ids // top_count
    send_x = jnp.where(is_live[:, None], tokens_in[token_ids], jnp.zeros((), tokens_in.dtype))
    send_dy = jnp.where(is_live[:, None], grad_out[token_ids], jnp.zeros((), grad_out.dtype))
    send_gate = jnp.where(
        is_live, gate_weights.reshape(-1)[safe_ids], jnp.zeros((), gate_weights.dtype)
    )
    lane_pad = 128
    gate_cols = jnp.zeros((device_count * capacity, lane_pad), send_x.dtype).at[:, 0].set(send_gate)
    outgoing = jnp.concatenate([send_x, send_dy, gate_cols], axis=1).reshape(
        device_count, capacity, 2 * model_width + lane_pad
    )
    arrived = lax.all_to_all(outgoing, ("zl", "core", "ep"), 0, 0, tiled=True).reshape(
        device_count * capacity, 2 * model_width + lane_pad
    )
    rows_x = arrived[:, :model_width]
    rows_dy = arrived[:, model_width : 2 * model_width]
    rows_gate = arrived[:, 2 * model_width]
    row_grad, gate_grad, part_in, part_down = expert_backward(
        rows_x, rows_dy, rows_gate, w_in, w_down
    )
    back_cols = jnp.zeros((device_count * capacity, lane_pad), row_grad.dtype).at[:, 0].set(gate_grad)
    returning = jnp.concatenate([row_grad, back_cols], axis=1).reshape(
        device_count, capacity, model_width + lane_pad
    )
    came_back = lax.all_to_all(returning, ("zl", "core", "ep"), 0, 0, tiled=True).reshape(
        device_count * capacity, model_width + lane_pad
    )[send_slot]
    grads_rows = came_back[:, :model_width]
    d_tokens = jnp.sum(
        grads_rows.reshape(tok_count, top_count, model_width).astype(jnp.float32), axis=1
    ).astype(jnp.bfloat16)
    d_gates = came_back[:, model_width].reshape(tok_count, top_count)
    core_count = lax.axis_size("core")
    core_index = lax.axis_index("core")
    group_index = lax.axis_index("zl") * core_count + core_index
    column_index = lax.axis_index("ep")
    partner_index = group_index - core_index + (core_count - 1 - core_index)
    own_slot = placement[group_index, column_index]
    partner_slot = placement[partner_index, column_index]
    hidden_width = part_down.shape[1]
    parts = jnp.concatenate([part_in, part_down], axis=1).astype(jnp.bfloat16)
    parts = parts.reshape(-1, core_count, model_width // group_count, parts.shape[1])
    own_rows = jnp.take(parts, core_index, axis=1)
    send_rows = jnp.take(parts, core_count - 1 - core_index, axis=1)
    got_rows = lax.ppermute(send_rows, "core", [(0, 1), (1, 0)])
    slots = jnp.arange(KPC, dtype=jnp.int32)
    own_mask = (slots == own_slot).astype(jnp.float32)[:, None, None, None]
    got_mask = (slots == partner_slot).astype(jnp.float32)[:, None, None, None]
    stacked = (
        own_mask * own_rows[None].astype(jnp.float32) + got_mask * got_rows[None].astype(jnp.float32)
    ).astype(jnp.bfloat16)
    summed = lax.psum_scatter(stacked, "zl", scatter_dimension=1, tiled=True)
    summed = summed.reshape(KPC, model_width // group_count, -1)
    width_in = summed.shape[2] - hidden_width
    return (d_tokens, d_gates, summed[:, :, :width_in], summed[:, :, width_in:])


def solution(mesh):
    grp_size = mesh.shape["grp"]
    core_size = 2
    split_mesh = jax.sharding.Mesh(
        mesh.devices.reshape(grp_size // core_size, core_size, mesh.shape["ep"]), ("zl", "core", "ep")
    )
    rows = ("zl", "core", "ep")
    placed = (
        P(rows, None),
        P(rows, None),
        P(rows, None),
        P(rows, None),
        P(),
        P(("zl", "core"), "ep", None, None),
        P(("zl", "core"), "ep", None, None),
    )
    return jax.shard_map(
        shards,
        mesh=split_mesh,
        in_specs=placed,
        out_specs=(
            P(rows, None),
            P(rows, None),
            P("ep", ("zl", "core"), None),
            P("ep", ("zl", "core"), None),
        ),
        check_vma=False,
    )
```

```python
import jax
import jax.numpy as jnp
from jax import lax
from jax.sharding import PartitionSpec as P

KPC = 2


def expert_backward(rows_x, rows_dy, rows_gate, w_in, w_down):
    hidden = w_down.shape[1]
    both = jnp.dot(rows_x, w_in, preferred_element_type=jnp.float32)
    gate_pre = both[:, :hidden]
    up_part = both[:, hidden:]
    sigmoid_gate = jax.nn.sigmoid(gate_pre)
    silu_gate = gate_pre * sigmoid_gate
    activation = (silu_gate * up_part).astype(jnp.bfloat16)
    out_rows = lax.dot_general(
        activation, w_down, (((1,), (1,)), ((), ())), preferred_element_type=jnp.float32
    )
    gate_grad = jnp.sum(rows_dy.astype(jnp.float32) * out_rows, axis=1).astype(jnp.bfloat16)
    out_grad = (rows_gate.astype(jnp.float32)[:, None] * rows_dy.astype(jnp.float32)).astype(
        jnp.bfloat16
    )
    act_grad = jnp.dot(out_grad, w_down, preferred_element_type=jnp.float32)
    gate_grad_pre = act_grad * up_part * sigmoid_gate * (1.0 + gate_pre * (1.0 - sigmoid_gate))
    up_grad = act_grad * silu_gate
    both_grad = jnp.concatenate([gate_grad_pre, up_grad], axis=1).astype(jnp.bfloat16)
    row_grad = lax.dot_general(
        both_grad, w_in, (((1,), (1,)), ((), ())), preferred_element_type=jnp.float32
    ).astype(jnp.bfloat16)
    part_in = lax.dot_general(
        rows_x, both_grad, (((0,), (0,)), ((), ())), preferred_element_type=jnp.float32
    )
    part_down = lax.dot_general(
        out_grad, activation, (((0,), (0,)), ((), ())), preferred_element_type=jnp.float32
    )
    return (row_grad, gate_grad, part_in, part_down)


def shards(tokens_in, grad_out, replica_of, gate_weights, placement, w_in_rep, w_down_rep):
    tok_count, model_width = tokens_in.shape
    top_count = replica_of.shape[1]
    group_count = lax.axis_size("zl") * lax.axis_size("core")
    lane_count = lax.axis_size("ep")
    device_count = group_count * lane_count
    capacity = max(2, 2 * tok_count * top_count // device_count)
    w_in = w_in_rep[0, 0]
    w_down = w_down_rep[0, 0]
    dest_rows = replica_of.reshape(-1)
    row_count = tok_count * top_count
    row_ids = jnp.arange(row_count, dtype=jnp.int32)
    earlier = (dest_rows[:, None] == dest_rows[None, :]) & (row_ids[None, :] < row_ids[:, None])
    rank_in = jnp.sum(earlier.astype(jnp.int32), axis=1)
    send_slot = dest_rows * capacity + rank_in
    slot_table = jnp.full((device_count * capacity,), -1, jnp.int32).at[send_slot].set(row_ids)
    is_live = slot_table >= 0
    safe_ids = jnp.maximum(slot_table, 0)
    slot_token = jnp.where(is_live, safe_ids // top_count, -1)
    pick_token = (slot_token[:, None] == jnp.arange(tok_count, dtype=jnp.int32)[None, :]).astype(
        tokens_in.dtype
    )
    send_x = jnp.dot(pick_token, tokens_in, preferred_element_type=tokens_in.dtype)
    send_dy = jnp.dot(pick_token, grad_out, preferred_element_type=grad_out.dtype)
    send_gate = jnp.where(
        is_live, gate_weights.reshape(-1)[safe_ids], jnp.zeros((), gate_weights.dtype)
    )
    lane_pad = 128
    gate_cols = jnp.zeros((device_count * capacity, lane_pad), send_x.dtype).at[:, 0].set(send_gate)
    outgoing = jnp.concatenate([send_x, send_dy, gate_cols], axis=1).reshape(
        device_count, capacity, 2 * model_width + lane_pad
    )
    arrived = lax.all_to_all(outgoing, ("zl", "core", "ep"), 0, 0, tiled=True).reshape(
        device_count * capacity, 2 * model_width + lane_pad
    )
    rows_x = arrived[:, :model_width]
    rows_dy = arrived[:, model_width : 2 * model_width]
    rows_gate = arrived[:, 2 * model_width]
    row_grad, gate_grad, part_in, part_down = expert_backward(
        rows_x, rows_dy, rows_gate, w_in, w_down
    )
    back_cols = jnp.zeros((device_count * capacity, lane_pad), row_grad.dtype).at[:, 0].set(gate_grad)
    returning = jnp.concatenate([row_grad, back_cols], axis=1).reshape(
        device_count, capacity, model_width + lane_pad
    )
    came_back = lax.all_to_all(returning, ("zl", "core", "ep"), 0, 0, tiled=True).reshape(
        device_count * capacity, model_width + lane_pad
    )
    slot_of_token = send_slot.reshape(tok_count, top_count)
    slot_ids = jnp.arange(device_count * capacity, dtype=jnp.int32)
    pick_slot = jnp.any(slot_of_token[:, :, None] == slot_ids[None, None, :], axis=1).astype(
        came_back.dtype
    )
    d_tokens = jnp.dot(
        pick_slot, came_back[:, :model_width], preferred_element_type=jnp.float32
    ).astype(jnp.bfloat16)
    d_gates = came_back[:, model_width][send_slot].reshape(tok_count, top_count)
    core_count = lax.axis_size("core")
    core_index = lax.axis_index("core")
    group_index = lax.axis_index("zl") * core_count + core_index
    column_index = lax.axis_index("ep")
    partner_index = group_index - core_index + (core_count - 1 - core_index)
    own_slot = placement[group_index, column_index]
    partner_slot = placement[partner_index, column_index]
    hidden_width = part_down.shape[1]
    parts = jnp.concatenate([part_in, part_down], axis=1).astype(jnp.bfloat16)
    parts = parts.reshape(-1, core_count, model_width // group_count, parts.shape[1])
    own_rows = jnp.take(parts, core_index, axis=1)
    send_rows = jnp.take(parts, core_count - 1 - core_index, axis=1)
    got_rows = lax.ppermute(send_rows, "core", [(0, 1), (1, 0)])
    slots = jnp.arange(KPC, dtype=jnp.int32)
    own_mask = (slots == own_slot).astype(jnp.float32)[:, None, None, None]
    got_mask = (slots == partner_slot).astype(jnp.float32)[:, None, None, None]
    stacked = (
        own_mask * own_rows[None].astype(jnp.float32) + got_mask * got_rows[None].astype(jnp.float32)
    ).astype(jnp.bfloat16)
    summed = lax.psum_scatter(stacked, "zl", scatter_dimension=1, tiled=True)
    summed = summed.reshape(KPC, model_width // group_count, -1)
    width_in = summed.shape[2] - hidden_width
    return (d_tokens, d_gates, summed[:, :, :width_in], summed[:, :, width_in:])


def solution(mesh):
    grp_size = mesh.shape["grp"]
    core_size = 2
    split_mesh = jax.sharding.Mesh(
        mesh.devices.reshape(grp_size // core_size, core_size, mesh.shape["ep"]), ("zl", "core", "ep")
    )
    rows = ("zl", "core", "ep")
    placed = (
        P(rows, None),
        P(rows, None),
        P(rows, None),
        P(rows, None),
        P(),
        P(("zl", "core"), "ep", None, None),
        P(("zl", "core"), "ep", None, None),
    )
    return jax.shard_map(
        shards,
        mesh=split_mesh,
        in_specs=placed,
        out_specs=(
            P(rows, None),
            P(rows, None),
            P("ep", ("zl", "core"), None),
            P("ep", ("zl", "core"), None),
        ),
        check_vma=False,
    )
```

```python
import jax
import jax.numpy as jnp
from jax import lax
from jax.sharding import PartitionSpec as P

KPC = 2


def expert_backward(rows_x, rows_dy, rows_gate, w_in, w_down):
    hidden = w_down.shape[1]
    both = jnp.dot(rows_x, w_in, preferred_element_type=jnp.float32)
    gate_pre = both[:, :hidden]
    up_part = both[:, hidden:]
    sigmoid_gate = jax.nn.sigmoid(gate_pre)
    silu_gate = gate_pre * sigmoid_gate
    activation = (silu_gate * up_part).astype(jnp.bfloat16)
    out_rows = lax.dot_general(
        activation, w_down, (((1,), (1,)), ((), ())), preferred_element_type=jnp.float32
    )
    gate_grad = jnp.sum(rows_dy.astype(jnp.float32) * out_rows, axis=1).astype(jnp.bfloat16)
    out_grad = (rows_gate.astype(jnp.float32)[:, None] * rows_dy.astype(jnp.float32)).astype(
        jnp.bfloat16
    )
    act_grad = jnp.dot(out_grad, w_down, preferred_element_type=jnp.float32)
    gate_grad_pre = act_grad * up_part * sigmoid_gate * (1.0 + gate_pre * (1.0 - sigmoid_gate))
    up_grad = act_grad * silu_gate
    both_grad = jnp.concatenate([gate_grad_pre, up_grad], axis=1).astype(jnp.bfloat16)
    row_grad = lax.dot_general(
        both_grad, w_in, (((1,), (1,)), ((), ())), preferred_element_type=jnp.float32
    ).astype(jnp.bfloat16)
    part_in = lax.dot_general(
        rows_x, both_grad, (((0,), (0,)), ((), ())), preferred_element_type=jnp.float32
    )
    part_down = lax.dot_general(
        out_grad, activation, (((0,), (0,)), ((), ())), preferred_element_type=jnp.float32
    )
    return (row_grad, gate_grad, part_in, part_down)


def shards(tokens_in, grad_out, replica_of, gate_weights, placement, w_in_rep, w_down_rep):
    tok_count, model_width = tokens_in.shape
    top_count = replica_of.shape[1]
    group_count = lax.axis_size("zl") * lax.axis_size("core")
    lane_count = lax.axis_size("ep")
    device_count = group_count * lane_count
    capacity = max(2, 2 * tok_count * top_count // device_count)
    w_in = w_in_rep[0, 0]
    w_down = w_down_rep[0, 0]
    dest_rows = replica_of.reshape(-1)
    row_count = tok_count * top_count
    row_ids = jnp.arange(row_count, dtype=jnp.int32)
    earlier = (dest_rows[:, None] == dest_rows[None, :]) & (row_ids[None, :] < row_ids[:, None])
    rank_in = jnp.sum(earlier.astype(jnp.int32), axis=1)
    send_slot = dest_rows * capacity + rank_in
    slot_table = jnp.full((device_count * capacity,), -1, jnp.int32).at[send_slot].set(row_ids)
    is_live = slot_table >= 0
    safe_ids = jnp.maximum(slot_table, 0)
    slot_token = jnp.where(is_live, safe_ids // top_count, -1)
    pick_token = (slot_token[:, None] == jnp.arange(tok_count, dtype=jnp.int32)[None, :]).astype(
        tokens_in.dtype
    )
    send_x = jnp.dot(pick_token, tokens_in, preferred_element_type=tokens_in.dtype)
    send_dy = jnp.dot(pick_token, grad_out, preferred_element_type=grad_out.dtype)
    send_gate = jnp.where(
        is_live, gate_weights.reshape(-1)[safe_ids], jnp.zeros((), gate_weights.dtype)
    )
    lane_pad = 128
    gate_cols = jnp.zeros((device_count * capacity, lane_pad), send_x.dtype).at[:, 0].set(send_gate)
    outgoing = jnp.concatenate([send_x, send_dy, gate_cols], axis=1).reshape(
        device_count, capacity, 2 * model_width + lane_pad
    )
    arrived = lax.all_to_all(outgoing, ("zl", "core", "ep"), 0, 0, tiled=True).reshape(
        device_count * capacity, 2 * model_width + lane_pad
    )
    rows_x = arrived[:, :model_width]
    rows_dy = arrived[:, model_width : 2 * model_width]
    rows_gate = arrived[:, 2 * model_width]
    row_grad, gate_grad, part_in, part_down = expert_backward(
        rows_x, rows_dy, rows_gate, w_in, w_down
    )
    back_cols = jnp.zeros((device_count * capacity, lane_pad), row_grad.dtype).at[:, 0].set(gate_grad)
    returning = jnp.concatenate([row_grad, back_cols], axis=1).reshape(
        device_count, capacity, model_width + lane_pad
    )
    came_back = lax.all_to_all(returning, ("zl", "core", "ep"), 0, 0, tiled=True).reshape(
        device_count * capacity, model_width + lane_pad
    )
    slot_of_token = send_slot.reshape(tok_count, top_count)
    slot_ids = jnp.arange(device_count * capacity, dtype=jnp.int32)
    pick_slot = jnp.any(slot_of_token[:, :, None] == slot_ids[None, None, :], axis=1).astype(
        came_back.dtype
    )
    d_tokens = jnp.dot(
        pick_slot, came_back[:, :model_width], preferred_element_type=jnp.float32
    ).astype(jnp.bfloat16)
    d_gates = came_back[:, model_width][send_slot].reshape(tok_count, top_count)
    core_count = lax.axis_size("core")
    core_index = lax.axis_index("core")
    group_index = lax.axis_index("zl") * core_count + core_index
    column_index = lax.axis_index("ep")
    partner_index = group_index - core_index + (core_count - 1 - core_index)
    own_slot = placement[group_index, column_index]
    partner_slot = placement[partner_index, column_index]
    slots = jnp.arange(KPC, dtype=jnp.int32)
    own_mask = (slots == own_slot).astype(jnp.float32)[:, None, None, None]
    got_mask = (slots == partner_slot).astype(jnp.float32)[:, None, None, None]

    def reduce_copies(part):
        part = part.astype(jnp.bfloat16).reshape(
            -1, core_count, model_width // group_count, part.shape[1]
        )
        own_rows = jnp.take(part, core_index, axis=1)
        send_rows = jnp.take(part, core_count - 1 - core_index, axis=1)
        got_rows = lax.ppermute(send_rows, "core", [(0, 1), (1, 0)])
        stacked = (
            own_mask * own_rows[None].astype(jnp.float32)
            + got_mask * got_rows[None].astype(jnp.float32)
        ).astype(jnp.bfloat16)
        summed = lax.psum_scatter(stacked, "zl", scatter_dimension=1, tiled=True)
        return summed.reshape(KPC, model_width // group_count, -1)

    summed_down = reduce_copies(part_down)
    summed_in = reduce_copies(part_in)
    return (d_tokens, d_gates, summed_in, summed_down)

def solution(mesh):
    grp_size = mesh.shape["grp"]
    core_size = 2
    split_mesh = jax.sharding.Mesh(
        mesh.devices.reshape(grp_size // core_size, core_size, mesh.shape["ep"]), ("zl", "core", "ep")
    )
    rows = ("zl", "core", "ep")
    placed = (
        P(rows, None),
        P(rows, None),
        P(rows, None),
        P(rows, None),
        P(),
        P(("zl", "core"), "ep", None, None),
        P(("zl", "core"), "ep", None, None),
    )
    return jax.shard_map(
        shards,
        mesh=split_mesh,
        in_specs=placed,
        out_specs=(
            P(rows, None),
            P(rows, None),
            P("ep", ("zl", "core"), None),
            P("ep", ("zl", "core"), None),
        ),
        check_vma=False,
    )
```

```python
import jax
import jax.numpy as jnp
from jax import lax
from jax.sharding import PartitionSpec as P

KPC = 2


def expert_backward(rows_x, rows_dy, rows_gate, w_in, w_down):
    hidden = w_down.shape[1]
    both = jnp.dot(rows_x, w_in, preferred_element_type=jnp.float32)
    gate_pre = both[:, :hidden]
    up_part = both[:, hidden:]
    sigmoid_gate = jax.nn.sigmoid(gate_pre)
    silu_gate = gate_pre * sigmoid_gate
    activation = (silu_gate * up_part).astype(jnp.bfloat16)
    out_rows = lax.dot_general(
        activation, w_down, (((1,), (1,)), ((), ())), preferred_element_type=jnp.float32
    )
    gate_grad = jnp.sum(rows_dy.astype(jnp.float32) * out_rows, axis=1).astype(jnp.bfloat16)
    out_grad = (rows_gate.astype(jnp.float32)[:, None] * rows_dy.astype(jnp.float32)).astype(
        jnp.bfloat16
    )
    act_grad = jnp.dot(out_grad, w_down, preferred_element_type=jnp.float32)
    gate_grad_pre = act_grad * up_part * sigmoid_gate * (1.0 + gate_pre * (1.0 - sigmoid_gate))
    up_grad = act_grad * silu_gate
    both_grad = jnp.concatenate([gate_grad_pre, up_grad], axis=1).astype(jnp.bfloat16)
    row_grad = lax.dot_general(
        both_grad, w_in, (((1,), (1,)), ((), ())), preferred_element_type=jnp.float32
    ).astype(jnp.bfloat16)
    part_in = lax.dot_general(
        rows_x, both_grad, (((0,), (0,)), ((), ())), preferred_element_type=jnp.float32
    )
    part_down = lax.dot_general(
        out_grad, activation, (((0,), (0,)), ((), ())), preferred_element_type=jnp.float32
    )
    return (row_grad, gate_grad, part_in, part_down)


def shards(tokens_in, grad_out, replica_of, gate_weights, placement, w_in_rep, w_down_rep):
    tok_count, model_width = tokens_in.shape
    top_count = replica_of.shape[1]
    group_count = lax.axis_size("zl") * lax.axis_size("core")
    lane_count = lax.axis_size("ep")
    device_count = group_count * lane_count
    capacity = max(2, 2 * tok_count * top_count // device_count)
    w_in = w_in_rep[0, 0]
    w_down = w_down_rep[0, 0]
    dest_rows = replica_of.reshape(-1)
    row_count = tok_count * top_count
    row_ids = jnp.arange(row_count, dtype=jnp.int32)
    earlier = (dest_rows[:, None] == dest_rows[None, :]) & (row_ids[None, :] < row_ids[:, None])
    rank_in = jnp.sum(earlier.astype(jnp.int32), axis=1)
    send_slot = dest_rows * capacity + rank_in
    slot_table = jnp.full((device_count * capacity,), -1, jnp.int32).at[send_slot].set(row_ids)
    is_live = slot_table >= 0
    safe_ids = jnp.maximum(slot_table, 0)
    slot_token = jnp.where(is_live, safe_ids // top_count, -1)
    pick_token = (slot_token[:, None] == jnp.arange(tok_count, dtype=jnp.int32)[None, :]).astype(
        tokens_in.dtype
    )
    send_x = jnp.dot(pick_token, tokens_in, preferred_element_type=tokens_in.dtype)
    send_dy = jnp.dot(pick_token, grad_out, preferred_element_type=grad_out.dtype)
    send_gate = jnp.where(
        is_live, gate_weights.reshape(-1)[safe_ids], jnp.zeros((), gate_weights.dtype)
    )
    lane_pad = 128
    gate_cols = jnp.zeros((device_count * capacity, lane_pad), send_x.dtype).at[:, 0].set(send_gate)
    outgoing = jnp.concatenate([send_x, send_dy, gate_cols], axis=1).reshape(
        device_count, capacity, 2 * model_width + lane_pad
    )
    arrived = lax.all_to_all(outgoing, ("zl", "core", "ep"), 0, 0, tiled=True).reshape(
        device_count * capacity, 2 * model_width + lane_pad
    )
    rows_x = arrived[:, :model_width]
    rows_dy = arrived[:, model_width : 2 * model_width]
    rows_gate = arrived[:, 2 * model_width]
    row_grad, gate_grad, part_in, part_down = expert_backward(
        rows_x, rows_dy, rows_gate, w_in, w_down
    )
    back_cols = jnp.zeros((device_count * capacity, lane_pad), row_grad.dtype).at[:, 0].set(gate_grad)
    returning = jnp.concatenate([row_grad, back_cols], axis=1).reshape(
        device_count, capacity, model_width + lane_pad
    )
    came_back = lax.all_to_all(returning, ("zl", "core", "ep"), 0, 0, tiled=True).reshape(
        device_count * capacity, model_width + lane_pad
    )
    slot_of_token = send_slot.reshape(tok_count, top_count)
    slot_ids = jnp.arange(device_count * capacity, dtype=jnp.int32)
    pick_slot = jnp.any(slot_of_token[:, :, None] == slot_ids[None, None, :], axis=1).astype(
        came_back.dtype
    )
    d_tokens = jnp.dot(
        pick_slot, came_back[:, :model_width], preferred_element_type=jnp.float32
    ).astype(jnp.bfloat16)
    d_gates = came_back[:, model_width][send_slot].reshape(tok_count, top_count)
    core_count = lax.axis_size("core")
    core_index = lax.axis_index("core")
    group_index = lax.axis_index("zl") * core_count + core_index
    column_index = lax.axis_index("ep")
    partner_index = group_index - core_index + (core_count - 1 - core_index)
    own_slot = placement[group_index, column_index]
    partner_slot = placement[partner_index, column_index]
    slots = jnp.arange(KPC, dtype=jnp.int32)
    own_mask = (slots == own_slot).astype(jnp.float32)[:, None, None, None]
    got_mask = (slots == partner_slot).astype(jnp.float32)[:, None, None, None]

    def reduce_copies(part, on_core):
        part = part.astype(jnp.bfloat16).reshape(
            -1, core_count, model_width // group_count, part.shape[1]
        )
        own_rows = jnp.take(part, core_index, axis=1)
        send_rows = jnp.take(part, core_count - 1 - core_index, axis=1)
        got_rows = lax.ppermute(send_rows, "core", [(0, 1), (1, 0)])
        stacked = (
            own_mask * own_rows[None].astype(jnp.float32)
            + got_mask * got_rows[None].astype(jnp.float32)
        ).astype(jnp.bfloat16)
        if on_core:
            gathered = lax.all_to_all(stacked, "zl", 1, 1, tiled=True)
            return jnp.sum(gathered.astype(jnp.float32), axis=1).astype(jnp.bfloat16)
        summed = lax.psum_scatter(stacked, "zl", scatter_dimension=1, tiled=True)
        return summed.reshape(KPC, model_width // group_count, -1)

    summed_down = reduce_copies(part_down, True)
    summed_in = reduce_copies(part_in, False)
    return (d_tokens, d_gates, summed_in, summed_down)

def solution(mesh):
    grp_size = mesh.shape["grp"]
    core_size = 2
    split_mesh = jax.sharding.Mesh(
        mesh.devices.reshape(grp_size // core_size, core_size, mesh.shape["ep"]), ("zl", "core", "ep")
    )
    rows = ("zl", "core", "ep")
    placed = (
        P(rows, None),
        P(rows, None),
        P(rows, None),
        P(rows, None),
        P(),
        P(("zl", "core"), "ep", None, None),
        P(("zl", "core"), "ep", None, None),
    )
    return jax.shard_map(
        shards,
        mesh=split_mesh,
        in_specs=placed,
        out_specs=(
            P(rows, None),
            P(rows, None),
            P("ep", ("zl", "core"), None),
            P("ep", ("zl", "core"), None),
        ),
        check_vma=False,
    )
```
